32 devices in a mesh: space: 4 (over y, core), energy: 8 (over z, x).
Axes of the slice: x: 2, y: 2, z: 4, core: 2. Of those that a mesh axis runs over, the one named last changes fastest.
Arguments:
- lesser: bfloat16 [8, 4, 3, 128, 256], P('energy', 'space'), may hold values from -6 to 6
- greater: bfloat16 [8, 4, 3, 128, 256], P('energy', 'space'), may hold values from -2.109375 to 2.109375
Outputs:
- polarization: float32 [8, 4, 3, 128, 256], P('energy', 'space')
The draws below stay inside these ranges and needn't reach their ends.
All inputs are finite; a program needn't handle non-finite values.
Results may differ from the reference program's by a relative error of at most 0.0003.
Values may be sent and summed in bfloat16 or wider, within the bound.
No kernel may reach another device: no remote copies, remote signals or barrier semaphores. Data moves between devices by JAX's collectives and lax.ppermute only.
A program may use at most 64 MiB of HBM per device.

```python
import jax
import jax.numpy as jnp
from jax import lax

BS = 128
NB = 4
NE = 8


def steps_of(rng, dims, pieces, low, high):
    gain = 1.0
    for position, shards_of in pieces:
        heights = jax.random.uniform(jax.random.fold_in(jax.random.fold_in(rng, 6), position), (shards_of,), jnp.float32, low / len(pieces), high / len(pieces))
        gain = gain * jnp.repeat(jnp.exp(heights), dims[position] // shards_of).reshape((-1,) + (1,) * (len(dims) - 1 - position))
    return gain


def gaussian(rng, dims, spread, most, cuts=(), held_as=jnp.bfloat16):
    loudness = steps_of(rng, dims, cuts, -0.22, 0.18) if cuts else 1.0
    values = jax.random.normal(rng, dims, jnp.float32) * spread * loudness
    return jnp.minimum(jnp.maximum(values, -most), most).astype(held_as)


def setup_inputs(seed: int = 0) -> dict:
    key_of = jax.random.split(jax.random.key(seed), 3)
    return {
        "lesser": gaussian(key_of[0], (NE, NB, 3, BS, 2 * BS), 1.0, 6.0, ((0, 8), (1, 4))),
        "greater": gaussian(key_of[1], (NE, NB, 3, BS, 2 * BS), (NE ** -0.5), 2.109375, ((0, 8), (1, 4))),
    }


def flip_tiles(tiles):
    shape = tiles.shape
    width = shape[-2]
    split = tiles.reshape(shape[:-1] + (2, width))
    turned = jnp.swapaxes(split, -3, -1)
    return turned.reshape(shape)


def mirror_all(greater):
    zero_tile = jnp.zeros_like(greater[:, :1, 0])
    below = jnp.concatenate([zero_tile, greater[:, :-1, 2]], axis=1)
    above = jnp.concatenate([greater[:, 1:, 0], zero_tile], axis=1)
    stacked = jnp.stack([below, greater[:, :, 1], above], axis=2)
    return flip_tiles(stacked)


def reference(lesser, greater):
    mirrored = mirror_all(greater)
    total = lesser.shape[0]
    width = lesser.shape[3]

    def one_row(pair):
        left, right = pair
        left = left.astype(jnp.float32)
        right = right.astype(jnp.float32)
        left_c = left[..., :width] + 1j * left[..., width:]
        right_c = right[..., :width] + 1j * right[..., width:]
        left_hat = jnp.fft.fft(left_c, axis=0)
        right_hat = jnp.fft.ifft(right_c, axis=0) * total
        result = jnp.fft.ifft(left_hat * right_hat, axis=0)
        return jnp.concatenate([jnp.real(result), jnp.imag(result)], axis=-1).astype(jnp.float32)

    rows = lax.map(one_row, (jnp.swapaxes(lesser, 0, 1), jnp.swapaxes(mirrored, 0, 1)))
    return jnp.swapaxes(rows, 0, 1)
```

```python
import jax
import jax.numpy as jnp
from jax import lax
from jax.sharding import PartitionSpec as P


def flip_tiles(tiles):
    shape = tiles.shape
    width = shape[-2]
    split = tiles.reshape(shape[:-1] + (2, width))
    turned = jnp.swapaxes(split, -3, -1)
    return turned.reshape(shape)


def mirror(greater):
    count = lax.axis_size("space")
    forward = [(i, i + 1) for i in range(count - 1)]
    backward = [(i + 1, i) for i in range(count - 1)]
    below = lax.ppermute(greater[2], "space", forward)
    above = lax.ppermute(greater[0], "space", backward)
    return flip_tiles(jnp.stack([below, greater[1], above]))


def correlate(left, right):
    total = left.shape[0]
    width = left.shape[-1] // 2
    left = left.astype(jnp.float32)
    right = right.astype(jnp.float32)
    lre = jnp.concatenate([left[..., :width]] * 2)
    lim = jnp.concatenate([left[..., width:]] * 2)
    rre = right[..., :width]
    rim = right[..., width:]
    outs = []
    for shift in range(total):
        a = lre[shift:shift + total]
        b = lim[shift:shift + total]
        pre = jnp.sum(a * rre - b * rim, axis=0)
        pim = jnp.sum(a * rim + b * rre, axis=0)
        outs.append(jnp.concatenate([pre, pim], axis=-1))
    return jnp.stack(outs)


def on_device(lesser, greater):
    own_lesser = lesser[:, 0]
    mirrored = mirror(greater[0, 0])[None]
    left = lax.all_to_all(own_lesser, "energy", split_axis=2, concat_axis=0, tiled=True)
    right = lax.all_to_all(mirrored, "energy", split_axis=2, concat_axis=0, tiled=True)
    summed = correlate(left, right)
    back = lax.all_to_all(summed, "energy", split_axis=0, concat_axis=2, tiled=True)
    return back[:, None]


def solution(mesh):
    return jax.shard_map(
        on_device,
        mesh=mesh,
        in_specs=(P("energy", "space", None, None, None), P("energy", "space", None, None, None)),
        out_specs=P("energy", "space", None, None, None),
        check_vma=False,
    )
```

```python
import jax
import jax.numpy as jnp
from jax import lax
from jax.sharding import PartitionSpec as P


def flip_tiles(tiles):
    shape = tiles.shape
    width = shape[-2]
    split = tiles.reshape(shape[:-1] + (2, width))
    turned = jnp.swapaxes(split, -3, -1)
    return turned.reshape(shape)


def mirror(greater):
    count = lax.axis_size("space")
    forward = [(i, i + 1) for i in range(count - 1)]
    backward = [(i + 1, i) for i in range(count - 1)]
    below = lax.ppermute(greater[2], "space", forward)
    above = lax.ppermute(greater[0], "space", backward)
    return flip_tiles(jnp.stack([below, greater[1], above]))


def correlate(left, right):
    total = left.shape[0]
    width = left.shape[-1] // 2
    left = left.astype(jnp.float32)
    right = right.astype(jnp.float32)
    lre = jnp.concatenate([left[..., :width]] * 2)
    lim = jnp.concatenate([left[..., width:]] * 2)
    rre = right[..., :width]
    rim = right[..., width:]
    outs = []
    for shift in range(total):
        a = lre[shift:shift + total]
        b = lim[shift:shift + total]
        pre = jnp.sum(a * rre - b * rim, axis=0)
        pim = jnp.sum(a * rim + b * rre, axis=0)
        outs.append(jnp.concatenate([pre, pim], axis=-1))
    return jnp.stack(outs)


def on_device(lesser, greater):
    count = lax.axis_size("space")
    forward = [(i, i + 1) for i in range(count - 1)]
    backward = [(i + 1, i) for i in range(count - 1)]
    both = jnp.stack([lesser[0, 0], flip_tiles(greater[0, 0])])[None]
    got = lax.all_to_all(both, "energy", split_axis=3, concat_axis=0, tiled=True)
    left = got[:, 0]
    turned = got[:, 1]
    below = lax.ppermute(turned[:, 2], "space", forward)
    above = lax.ppermute(turned[:, 0], "space", backward)
    right = jnp.stack([below, turned[:, 1], above], axis=1)
    summed = correlate(left, right)
    back = lax.all_to_all(summed, "energy", split_axis=0, concat_axis=2, tiled=True)
    return back[:, None]


def solution(mesh):
    return jax.shard_map(
        on_device,
        mesh=mesh,
        in_specs=(P("energy", "space", None, None, None), P("energy", "space", None, None, None)),
        out_specs=P("energy", "space", None, None, None),
        check_vma=False,
    )
```

```python
import functools
import jax
import jax.numpy as jnp
from jax import lax
from jax.experimental import pallas as pl
from jax.experimental.pallas import tpu as pltpu
from jax.sharding import PartitionSpec as P


def flip_tiles(tiles):
    shape = tiles.shape
    width = shape[-2]
    split = tiles.reshape(shape[:-1] + (2, width))
    turned = jnp.swapaxes(split, -3, -1)
    return turned.reshape(shape)


def mirror(greater):
    count = lax.axis_size("space")
    forward = [(i, i + 1) for i in range(count - 1)]
    backward = [(i + 1, i) for i in range(count - 1)]
    below = lax.ppermute(greater[2], "space", forward)
    above = lax.ppermute(greater[0], "space", backward)
    return flip_tiles(jnp.stack([below, greater[1], above]))


def correlate(left, right):
    total = left.shape[0]
    width = left.shape[-1] // 2
    left = left.astype(jnp.float32)
    right = right.astype(jnp.float32)
    lre = jnp.concatenate([left[..., :width]] * 2)
    lim = jnp.concatenate([left[..., width:]] * 2)
    rre = right[..., :width]
    rim = right[..., width:]
    outs = []
    for shift in range(total):
        a = lre[shift:shift + total]
        b = lim[shift:shift + total]
        pre = jnp.sum(a * rre - b * rim, axis=0)
        pim = jnp.sum(a * rim + b * rre, axis=0)
        outs.append(jnp.concatenate([pre, pim], axis=-1))
    return jnp.stack(outs)


def pack_kernel(total, rows, lesser_ref, greater_ref, out_ref):
    tiles, height, width = lesser_ref.shape
    half = width // 2
    for tile in range(tiles):
        blocks = [
            greater_ref[tiles - 1 - tile, :, part * half:(part + 1) * half].astype(jnp.float32).T.astype(out_ref.dtype)
            for part in range(2)
        ]
        for chunk in range(total):
            low = max(tile * height, chunk * rows)
            high = min((tile + 1) * height, (chunk + 1) * rows)
            if low >= high:
                continue
            dst = slice(low - chunk * rows, high - chunk * rows)
            src = slice(low - tile * height, high - tile * height)
            out_ref[chunk, 0, dst, :] = lesser_ref[tile, src, :]
            for part in range(2):
                out_ref[chunk, 1, dst, part * half:(part + 1) * half] = blocks[part][src]


def pack(lesser, greater, total, rows):
    tiles, height, width = lesser.shape
    return pl.pallas_call(
        functools.partial(pack_kernel, total, rows),
        out_shape=jax.ShapeDtypeStruct((total, 2, rows, width), lesser.dtype),
        in_specs=[pl.BlockSpec(memory_space=pltpu.VMEM)] * 2,
        out_specs=pl.BlockSpec(memory_space=pltpu.VMEM),
        cost_estimate=pl.CostEstimate(flops=0, transcendentals=0, bytes_accessed=4 * lesser.size * 2),
    )(lesser, greater)


def pack_plain(lesser, greater, total, rows):
    width = lesser.shape[-1]
    turned = flip_tiles(greater)
    placed = jnp.stack([turned[2], turned[1], turned[0]])
    return jnp.stack([lesser.reshape(total, rows, width), placed.reshape(total, rows, width)], axis=1)


def on_device(lesser, greater):
    count = lax.axis_size("space")
    total = lax.axis_size("energy")
    forward = [(i, i + 1) for i in range(count - 1)]
    backward = [(i + 1, i) for i in range(count - 1)]
    tiles, height, width = lesser.shape[2:]
    rows = tiles * height // total
    if rows % 16 == 0 and height % 16 == 0:
        both = pack(lesser[0, 0], greater[0, 0], total, rows)
    else:
        both = pack_plain(lesser[0, 0], greater[0, 0], total, rows)
    got = lax.all_to_all(both, "energy", split_axis=0, concat_axis=0, tiled=True)
    left = got[:, 0]
    mine = got[:, 1]
    below = lax.ppermute(mine, "space", forward)
    above = lax.ppermute(mine, "space", backward)
    first = lax.axis_index("energy") * rows
    tile = (first + lax.broadcasted_iota(jnp.int32, (1, rows, 1), 1)) // height
    right = jnp.where(tile == 0, below, jnp.where(tile == 1, mine, above))
    summed = correlate(left, right)
    back = lax.all_to_all(summed, "energy", split_axis=0, concat_axis=0, tiled=True)
    return back.reshape((1, 1, tiles, height, width))


def solution(mesh):
    return jax.shard_map(
        on_device,
        mesh=mesh,
        in_specs=(P("energy", "space", None, None, None), P("energy", "space", None, None, None)),
        out_specs=P("energy", "space", None, None, None),
        check_vma=False,
    )
```

```python
import functools
import jax
import jax.numpy as jnp
from jax import lax
from jax.experimental import pallas as pl
from jax.experimental.pallas import tpu as pltpu
from jax.sharding import PartitionSpec as P


def flip_tiles(tiles):
    shape = tiles.shape
    width = shape[-2]
    split = tiles.reshape(shape[:-1] + (2, width))
    turned = jnp.swapaxes(split, -3, -1)
    return turned.reshape(shape)


def mirror(greater):
    count = lax.axis_size("space")
    forward = [(i, i + 1) for i in range(count - 1)]
    backward = [(i + 1, i) for i in range(count - 1)]
    below = lax.ppermute(greater[2], "space", forward)
    above = lax.ppermute(greater[0], "space", backward)
    return flip_tiles(jnp.stack([below, greater[1], above]))


def correlate(left, right):
    total = left.shape[0]
    width = left.shape[-1] // 2
    left = left.astype(jnp.float32)
    right = right.astype(jnp.float32)
    lre = jnp.concatenate([left[..., :width]] * 2)
    lim = jnp.concatenate([left[..., width:]] * 2)
    rre = right[..., :width]
    rim = right[..., width:]
    outs = []
    for shift in range(total):
        a = lre[shift:shift + total]
        b = lim[shift:shift + total]
        pre = jnp.sum(a * rre - b * rim, axis=0)
        pim = jnp.sum(a * rim + b * rre, axis=0)
        outs.append(jnp.concatenate([pre, pim], axis=-1))
    return jnp.stack(outs)


def pack_kernel(total, rows, lesser_ref, greater_ref, out_ref):
    tiles, height, width = lesser_ref.shape
    half = width // 2
    for tile in range(tiles):
        blocks = [
            greater_ref[tiles - 1 - tile, :, part * half:(part + 1) * half].astype(jnp.float32).T.astype(out_ref.dtype)
            for part in range(2)
        ]
        for chunk in range(total):
            low = max(tile * height, chunk * rows)
            high = min((tile + 1) * height, (chunk + 1) * rows)
            if low >= high:
                continue
            dst = slice(low - chunk * rows, high - chunk * rows)
            src = slice(low - tile * height, high - tile * height)
            out_ref[chunk, 0, dst, :] = lesser_ref[tile, src, :]
            for part in range(2):
                out_ref[chunk, 1, dst, part * half:(part + 1) * half] = blocks[part][src]


def pack(lesser, greater, total, rows):
    tiles, height, width = lesser.shape
    return pl.pallas_call(
        functools.partial(pack_kernel, total, rows),
        out_shape=jax.ShapeDtypeStruct((total, 2, rows, width), lesser.dtype),
        in_specs=[pl.BlockSpec(memory_space=pltpu.VMEM)] * 2,
        out_specs=pl.BlockSpec(memory_space=pltpu.VMEM),
        cost_estimate=pl.CostEstimate(flops=0, transcendentals=0, bytes_accessed=4 * lesser.size * 2),
    )(lesser, greater)


def pack_plain(lesser, greater, total, rows):
    width = lesser.shape[-1]
    turned = flip_tiles(greater)
    placed = jnp.stack([turned[2], turned[1], turned[0]])
    return jnp.stack([lesser.reshape(total, rows, width), placed.reshape(total, rows, width)], axis=1)


def wire_scale(total):
    bound = total * 2 * 6.0 * 2.109375
    scale = 1.0
    while bound * scale * 2 <= 65504.0:
        scale *= 2
    return scale


def on_device(lesser, greater):
    count = lax.axis_size("space")
    total = lax.axis_size("energy")
    forward = [(i, i + 1) for i in range(count - 1)]
    backward = [(i + 1, i) for i in range(count - 1)]
    tiles, height, width = lesser.shape[2:]
    rows = tiles * height // total
    if rows % 16 == 0 and height % 16 == 0:
        both = pack(lesser[0, 0], greater[0, 0], total, rows)
    else:
        both = pack_plain(lesser[0, 0], greater[0, 0], total, rows)
    got = lax.all_to_all(both, "energy", split_axis=0, concat_axis=0, tiled=True)
    left = got[:, 0]
    mine = got[:, 1]
    below = lax.ppermute(mine, "space", forward)
    above = lax.ppermute(mine, "space", backward)
    first = lax.axis_index("energy") * rows
    tile = (first + lax.broadcasted_iota(jnp.int32, (1, rows, 1), 1)) // height
    right = jnp.where(tile == 0, below, jnp.where(tile == 1, mine, above))
    summed = correlate(left, right)
    scale = wire_scale(total)
    packed = (summed * scale).astype(jnp.float16)
    back = lax.all_to_all(packed, "energy", split_axis=0, concat_axis=0, tiled=True)
    return (back.astype(jnp.float32) * (1.0 / scale)).reshape((1, 1, tiles, height, width))


def solution(mesh):
    return jax.shard_map(
        on_device,
        mesh=mesh,
        in_specs=(P("energy", "space", None, None, None), P("energy", "space", None, None, None)),
        out_specs=P("energy", "space", None, None, None),
        check_vma=False,
    )
```

```python
import functools
import jax
import jax.numpy as jnp
from jax import lax
from jax.experimental import pallas as pl
from jax.experimental.pallas import tpu as pltpu
from jax.sharding import PartitionSpec as P


def flip_tiles(tiles):
    shape = tiles.shape
    width = shape[-2]
    split = tiles.reshape(shape[:-1] + (2, width))
    turned = jnp.swapaxes(split, -3, -1)
    return turned.reshape(shape)


def mirror(greater):
    count = lax.axis_size("space")
    below = lax.ppermute(greater[2], "space", forward)
    above = lax.ppermute(greater[0], "space", backward)
    return flip_tiles(jnp.stack([below, greater[1], above]))


def correlate(left, right):
    total = left.shape[0]
    width = left.shape[-1] // 2
    left = left.astype(jnp.float32)
    right = right.astype(jnp.float32)
    lre = jnp.concatenate([left[..., :width]] * 2)
    lim = jnp.concatenate([left[..., width:]] * 2)
    rre = right[..., :width]
    rim = right[..., width:]
    outs = []
    for shift in range(total):
        a = lre[shift:shift + total]
        b = lim[shift:shift + total]
        pre = jnp.sum(a * rre - b * rim, axis=0)
        pim = jnp.sum(a * rim + b * rre, axis=0)
        outs.append(jnp.concatenate([pre, pim], axis=-1))
    return jnp.stack(outs)


def pack_kernel(total, rows, lesser_ref, greater_ref, out_ref):
    tiles, height, width = lesser_ref.shape
    half = width // 2
    for tile in range(tiles):
        blocks = [
            greater_ref[tiles - 1 - tile, :, part * half:(part + 1) * half].astype(jnp.float32).T.astype(out_ref.dtype)
            for part in range(2)
        ]
        for chunk in range(total):
            low = max(tile * height, chunk * rows)
            high = min((tile + 1) * height, (chunk + 1) * rows)
            if low >= high:
                continue
            dst = slice(low - chunk * rows, high - chunk * rows)
            src = slice(low - tile * height, high - tile * height)
            out_ref[chunk, 0, dst, :] = lesser_ref[tile, src, :]
            for part in range(2):
                out_ref[chunk, 1, dst, part * half:(part + 1) * half] = blocks[part][src]


def pack(lesser, greater, total, rows):
    tiles, height, width = lesser.shape
    return pl.pallas_call(
        functools.partial(pack_kernel, total, rows),
        out_shape=jax.ShapeDtypeStruct((total, 2, rows, width), lesser.dtype),
        in_specs=[pl.BlockSpec(memory_space=pltpu.VMEM)] * 2,
        out_specs=pl.BlockSpec(memory_space=pltpu.VMEM),
        cost_estimate=pl.CostEstimate(flops=0, transcendentals=0, bytes_accessed=4 * lesser.size * 2),
    )(lesser, greater)


def pack_plain(lesser, greater, total, rows):
    width = lesser.shape[-1]
    turned = flip_tiles(greater)
    placed = jnp.stack([turned[2], turned[1], turned[0]])
    return jnp.stack([lesser.reshape(total, rows, width), placed.reshape(total, rows, width)], axis=1)


def on_device(lesser, greater):
    count = lax.axis_size("space")
    total = lax.axis_size("energy")
    tiles, height, width = lesser.shape[2:]
    rows = tiles * height // total
    if rows % 16 == 0 and height % 16 == 0:
        both = pack(lesser[0, 0], greater[0, 0], total, rows)
    else:
        both = pack_plain(lesser[0, 0], greater[0, 0], total, rows)
    got = lax.all_to_all(both, "energy", split_axis=0, concat_axis=0, tiled=True)
    left = got[:, 0]
    mine = got[:, 1]
    inner = [(i, i ^ 1) for i in range(count) if i ^ 1 < count]
    outer = [(i, j) for i in range(1, count) for j in (i - 1, i + 1) if (i % 2 == 1) == (j == i + 1) and 0 <= j < count]
    near = lax.ppermute(mine, "space", inner)
    far = lax.ppermute(mine, "space", outer)
    odd = lax.axis_index("space") % 2 == 1
    below = jnp.where(odd, near, far)
    above = jnp.where(odd, far, near)
    first = lax.axis_index("energy") * rows
    tile = (first + lax.broadcasted_iota(jnp.int32, (1, rows, 1), 1)) // height
    right = jnp.where(tile == 0, below, jnp.where(tile == 1, mine, above))
    summed = correlate(left, right)
    back = lax.all_to_all(summed, "energy", split_axis=0, concat_axis=0, tiled=True)
    return back.reshape((1, 1, tiles, height, width))


def solution(mesh):
    return jax.shard_map(
        on_device,
        mesh=mesh,
        in_specs=(P("energy", "space", None, None, None), P("energy", "space", None, None, None)),
        out_specs=P("energy", "space", None, None, None),
        check_vma=False,
    )
```

```python
import functools
import jax
import jax.numpy as jnp
from jax import lax
from jax.experimental import pallas as pl
from jax.experimental.pallas import tpu as pltpu
from jax.sharding import PartitionSpec as P


def flip_tiles(tiles):
    shape = tiles.shape
    width = shape[-2]
    split = tiles.reshape(shape[:-1] + (2, width))
    turned = jnp.swapaxes(split, -3, -1)
    return turned.reshape(shape)


def correlate(left, right):
    total = left.shape[0]
    width = left.shape[-1] // 2
    left = left.astype(jnp.float32)
    right = right.astype(jnp.float32)
    lre = jnp.concatenate([left[..., :width]] * 2)
    lim = jnp.concatenate([left[..., width:]] * 2)
    rre = right[..., :width]
    rim = right[..., width:]
    outs = []
    for shift in range(total):
        a = lre[shift:shift + total]
        b = lim[shift:shift + total]
        pre = jnp.sum(a * rre - b * rim, axis=0)
        pim = jnp.sum(a * rim + b * rre, axis=0)
        outs.append(jnp.concatenate([pre, pim], axis=-1))
    return jnp.stack(outs)


def pack_kernel(total, rows, lesser_ref, greater_ref, out_ref):
    tiles, height, width = lesser_ref.shape
    half = width // 2
    for tile in range(tiles):
        blocks = [
            greater_ref[tiles - 1 - tile, :, part * half:(part + 1) * half].astype(jnp.float32).T.astype(out_ref.dtype)
            for part in range(2)
        ]
        for chunk in range(total):
            low = max(tile * height, chunk * rows)
            high = min((tile + 1) * height, (chunk + 1) * rows)
            if low >= high:
                continue
            dst = slice(low - chunk * rows, high - chunk * rows)
            src = slice(low - tile * height, high - tile * height)
            out_ref[chunk, 0, dst, :] = lesser_ref[tile, src, :]
            for part in range(2):
                out_ref[chunk, 1, dst, part * half:(part + 1) * half] = blocks[part][src]


def pack(lesser, greater, total, rows):
    tiles, height, width = lesser.shape
    return pl.pallas_call(
        functools.partial(pack_kernel, total, rows),
        out_shape=jax.ShapeDtypeStruct((total, 2, rows, width), lesser.dtype),
        in_specs=[pl.BlockSpec(memory_space=pltpu.VMEM)] * 2,
        out_specs=pl.BlockSpec(memory_space=pltpu.VMEM),
        cost_estimate=pl.CostEstimate(flops=0, transcendentals=0, bytes_accessed=4 * lesser.size * 2),
    )(lesser, greater)


def pack_plain(lesser, greater, total, rows):
    width = lesser.shape[-1]
    turned = flip_tiles(greater)
    placed = jnp.stack([turned[2], turned[1], turned[0]])
    return jnp.stack([lesser.reshape(total, rows, width), placed.reshape(total, rows, width)], axis=1)


def on_device(lesser, greater):
    count = lax.axis_size("space")
    total = lax.axis_size("energy")
    tiles, height, width = lesser.shape[2:]
    rows = tiles * height // total
    if rows % 16 == 0 and height % 16 == 0:
        both = pack(lesser[0, 0], greater[0, 0], total, rows)
    else:
        both = pack_plain(lesser[0, 0], greater[0, 0], total, rows)
    got = lax.all_to_all(both, "energy", split_axis=0, concat_axis=0, tiled=True)
    left = got[:, 0]
    mine = got[:, 1]
    inner = [(i, i ^ 1) for i in range(count) if i ^ 1 < count]
    outer = [(i, j) for i in range(1, count) for j in (i - 1, i + 1) if (i % 2 == 1) == (j == i + 1) and 0 <= j < count]
    near = lax.ppermute(mine, "space", inner)
    far = lax.ppermute(mine, "space", outer)
    odd = lax.axis_index("space") % 2 == 1
    below = jnp.where(odd, near, far)
    above = jnp.where(odd, far, near)
    first = lax.axis_index("energy") * rows
    tile = (first + lax.broadcasted_iota(jnp.int32, (1, rows, 1), 1)) // height
    right = jnp.where(tile == 0, below, jnp.where(tile == 1, mine, above))
    summed = correlate(left, right)
    back = lax.all_to_all(summed, "energy", split_axis=0, concat_axis=0, tiled=True)
    return back.reshape((1, 1, tiles, height, width))


def solution(mesh):
    return jax.shard_map(
        on_device,
        mesh=mesh,
        in_specs=(P("energy", "space", None, None, None), P("energy", "space", None, None, None)),
        out_specs=P("energy", "space", None, None, None),
        check_vma=False,
    )
```

```python
import functools
import jax
import jax.numpy as jnp
from jax import lax
from jax.experimental import pallas as pl
from jax.experimental.pallas import tpu as pltpu
from jax.sharding import PartitionSpec as P


def flip_tiles(tiles):
    shape = tiles.shape
    width = shape[-2]
    split = tiles.reshape(shape[:-1] + (2, width))
    turned = jnp.swapaxes(split, -3, -1)
    return turned.reshape(shape)


def correlate(left, right):
    total = left.shape[0]
    width = left.shape[-1] // 2
    left = left.astype(jnp.float32)
    right = right.astype(jnp.float32)
    lre = jnp.concatenate([left[..., :width]] * 2)
    lim = jnp.concatenate([left[..., width:]] * 2)
    rre = right[..., :width]
    rim = right[..., width:]
    outs = []
    for shift in range(total):
        a = lre[shift:shift + total]
        b = lim[shift:shift + total]
        pre = jnp.sum(a * rre - b * rim, axis=0)
        pim = jnp.sum(a * rim + b * rre, axis=0)
        outs.append(jnp.concatenate([pre, pim], axis=-1))
    return jnp.stack(outs)


def pack_kernel(total, rows, lesser_ref, greater_ref, out_ref):
    tiles, height, width = lesser_ref.shape
    half = width // 2
    for tile in range(tiles):
        blocks = [greater_ref[tile, :, part * half:(part + 1) * half].T for part in range(2)]
        for chunk in range(total):
            span = slice(chunk * rows, (chunk + 1) * rows)
            out_ref[chunk, 0, tile] = lesser_ref[tile, span, :]
            for part in range(2):
                out_ref[chunk, 1, tile, :, part * half:(part + 1) * half] = blocks[part][span]


def pack(lesser, greater, total, rows):
    tiles, height, width = lesser.shape
    return pl.pallas_call(
        functools.partial(pack_kernel, total, rows),
        out_shape=jax.ShapeDtypeStruct((total, 2, tiles, rows, width), lesser.dtype),
        in_specs=[pl.BlockSpec(memory_space=pltpu.VMEM)] * 2,
        out_specs=pl.BlockSpec(memory_space=pltpu.VMEM),
        cost_estimate=pl.CostEstimate(flops=0, transcendentals=0, bytes_accessed=4 * lesser.size * 2),
    )(lesser, greater)


def pack_plain(lesser, greater, total, rows):
    tiles, height, width = lesser.shape
    both = jnp.stack([lesser, flip_tiles(greater)])
    return jnp.swapaxes(both.reshape(2, tiles, total, rows, width), 0, 2).swapaxes(1, 2)


def on_device(lesser, greater):
    count = lax.axis_size("space")
    total = lax.axis_size("energy")
    tiles, height, width = lesser.shape[2:]
    rows = height // total
    if rows % 16 == 0:
        both = pack(lesser[0, 0], greater[0, 0], total, rows)
    else:
        both = pack_plain(lesser[0, 0], greater[0, 0], total, rows)
    got = lax.all_to_all(both, "energy", split_axis=0, concat_axis=0, tiled=True)
    left = got[:, 0]
    turned = got[:, 1]
    odd = lax.axis_index("space") % 2 == 1
    inner = [(i, i ^ 1) for i in range(count) if i ^ 1 < count]
    outer = [(i, j) for i in range(1, count) for j in (i - 1, i + 1) if (i % 2 == 1) == (j == i + 1) and 0 <= j < count]
    near = lax.ppermute(jnp.where(odd, turned[:, 0], turned[:, 2]), "space", inner)
    far = lax.ppermute(jnp.where(odd, turned[:, 2], turned[:, 0]), "space", outer)
    below = jnp.where(odd, near, far)
    above = jnp.where(odd, far, near)
    right = jnp.stack([below, turned[:, 1], above], axis=1)
    summed = correlate(left, right)
    back = lax.all_to_all(summed, "energy", split_axis=0, concat_axis=0, tiled=True)
    return jnp.swapaxes(back, 0, 1).reshape((1, 1, tiles, height, width))


def solution(mesh):
    return jax.shard_map(
        on_device,
        mesh=mesh,
        in_specs=(P("energy", "space", None, None, None), P("energy", "space", None, None, None)),
        out_specs=P("energy", "space", None, None, None),
        check_vma=False,
    )
```
